32 devices in a mesh: row: 8 (over y, x, core), col: 4 (over z).
Axes of the slice: x: 2, y: 2, z: 4, core: 2. Of those that a mesh axis runs over, the one named last changes fastest.
Arguments:
- a_blocks: bfloat16 [8, 4, 64, 128, 128], P('row', 'col'), may hold values from -6 to 6
- b_blocks: bfloat16 [8, 4, 2, 24, 128, 128], P('row', 'col'), may hold values from -0.1796875 to 0.1796875
- a_index: int32 [8, 4, 8, 192], P('row', 'col'), may hold values from 0 to 63
- b_index: int32 [8, 4, 8, 192], P('row', 'col'), may hold values from 0 to 23
- c_index: int32 [8, 4, 8, 192], P('row', 'col'), may hold values from 0 to 63
- pair_count: int32 [8, 4, 8], P('row', 'col'), may hold values from 1 to 192, as said below
Outputs:
- c_blocks: bfloat16 [8, 4, 64, 128, 128], P('row', 'col')
The draws below stay inside these ranges and needn't reach their ends.
Inputs may be any that keep to these rules, and one draw needn't show every extreme that they name: Only the first pair_count entries of each list are used; in every tick some C panel has all 192 entries live.
All inputs are finite; a program needn't handle non-finite values.
Results may differ from the reference program's by a relative error of at most 0.008.
Values may be sent and summed in bfloat16 or wider, within the bound.
No kernel may reach another device: no remote copies, remote signals or barrier semaphores. Data moves between devices by JAX's collectives and lax.ppermute only.
A program may use at most 192 MiB of HBM per device.

```python
import jax
import jax.numpy as jnp
from jax import lax

BS = 128
SLOTS_A = 64
SLOTS_B = 24
PAIRS = 192
SLOTS_C = 64
TICKS = 8
LOW = 3
HALVES = 2
N_ROW = 8
N_COL = 4


def draw_pair_count(key, part):
    first_key = jax.random.fold_in(key, 11)
    second_key = jax.random.fold_in(key, 23)
    busy_key = jax.random.fold_in(key, 37)
    shape = (N_ROW, N_COL, TICKS)
    first = jax.random.randint(first_key, shape, 1, PAIRS + 1)
    second = jax.random.randint(second_key, shape, 1, PAIRS + 1)
    counts = jnp.maximum(first * second // PAIRS, 1)
    busy = jax.random.randint(busy_key, (TICKS,), 0, N_ROW * N_COL)
    flat = jnp.arange(N_ROW * N_COL, dtype=jnp.int32).reshape(N_ROW, N_COL, 1)
    counts = jnp.where(flat == busy[None, None, :], PAIRS, counts)
    return counts.astype(jnp.int32)


def touch_ends(array, rng, smallest, largest):
    dims = array.shape
    index_at = [jax.random.randint(jax.random.fold_in(rng, axis), (), 0, dims[axis]) for axis in range(len(dims))]
    array = array.at[tuple(index_at)].set(smallest)
    longest = dims.index(max(dims))
    index_at[longest] = (index_at[longest] + 1) % dims[longest]
    return array.at[tuple(index_at)].set(largest)


def levels(rng, dims, cuts, least, high):
    loudness = 1.0
    for dim, shards_of in cuts:
        draws = jax.random.uniform(jax.random.fold_in(jax.random.fold_in(rng, 6), dim), (shards_of,), jnp.float32, least / len(cuts), high / len(cuts))
        loudness = loudness * jnp.repeat(jnp.exp(draws), dims[dim] // shards_of).reshape((-1,) + (1,) * (len(dims) - 1 - dim))
    return loudness


def scatter_about(stream_key, extent, scale, reach, split=(), kind=jnp.bfloat16):
    entries = scale * jax.random.normal(stream_key, extent, jnp.float32)
    if split:
        entries = entries * levels(stream_key, extent, split, -0.22, 0.18)
    return jnp.clip(entries, -reach, reach).astype(kind)


def setup_inputs(seed: int = 0) -> dict:
    streams_of = jax.random.split(jax.random.key(seed), 7)
    a_blocks = scatter_about(streams_of[0], (N_ROW, N_COL, SLOTS_A, BS, BS), 1.0, 6.0, ((0, 8), (1, 4)))
    b_blocks = scatter_about(streams_of[1], (N_ROW, N_COL, HALVES, SLOTS_B, BS, BS), 0.03, 0.1796875, ((0, 8), (1, 4)))
    a_index = touch_ends(jax.random.randint(streams_of[2], (N_ROW, N_COL, TICKS, PAIRS), 0, SLOTS_A), jax.random.fold_in(streams_of[2], 1), 0, SLOTS_A - 1).astype(jnp.int32)
    b_index = touch_ends(jax.random.randint(streams_of[3], (N_ROW, N_COL, TICKS, PAIRS), 0, SLOTS_B), jax.random.fold_in(streams_of[3], 1), 0, SLOTS_B - 1).astype(jnp.int32)
    c_index = touch_ends(jax.random.randint(streams_of[4], (N_ROW, N_COL, TICKS, PAIRS), 0, SLOTS_C), jax.random.fold_in(streams_of[4], 1), 0, SLOTS_C - 1).astype(jnp.int32)
    pair_count = draw_pair_count(jax.random.fold_in(streams_of[6], 71), 0)
    return {"a_blocks": a_blocks, "b_blocks": b_blocks, "a_index": a_index, "b_index": b_index, "c_index": c_index, "pair_count": pair_count}


def panel_blocks(a_blocks, b_blocks, a_index, b_index, c_index, pair_count, row_index, col_index):
    running = jnp.zeros((SLOTS_C, BS, BS), jnp.float32)
    positions = jnp.arange(PAIRS, dtype=jnp.int32)
    for tick in range(TICKS):
        offset = tick - LOW
        a_panel = a_blocks[(row_index + offset) % N_ROW, col_index]
        half_index = ((row_index + col_index + offset) % N_ROW) // N_COL
        b_panel = b_blocks[row_index, (col_index + offset) % N_COL, half_index]
        a_rows = a_panel[a_index[row_index, col_index, tick]].astype(jnp.float32)
        b_rows = b_panel[b_index[row_index, col_index, tick]].astype(jnp.float32)
        products = jnp.einsum("pik,pjk->pij", a_rows, b_rows)
        live_mask = (positions < pair_count[row_index, col_index, tick]).astype(jnp.float32)
        running = running.at[c_index[row_index, col_index, tick]].add(products * live_mask[:, None, None])
    return running.astype(jnp.bfloat16)


def reference(a_blocks, b_blocks, a_index, b_index, c_index, pair_count):
    devices = jnp.arange(N_ROW * N_COL, dtype=jnp.int32)

    def one_panel(device):
        return panel_blocks(a_blocks, b_blocks, a_index, b_index, c_index, pair_count, device // N_COL, device % N_COL)

    result = lax.map(one_panel, devices)
    return result.reshape(N_ROW, N_COL, SLOTS_C, BS, BS)
```

```python
import functools

import jax
import jax.numpy as jnp
from jax import lax
from jax.experimental import pallas as pl
from jax.experimental.pallas import tpu as pltpu
from jax.sharding import PartitionSpec as P


def passed_along(value, axis, steps):
    count = lax.axis_size(axis)
    pairs = [(source, (source + steps) % count) for source in range(count)]
    return lax.ppermute(value, axis, pairs)


def tick_kernel(first, last, count_ref, a_list, b_list, c_list, a_ref, b_ref, *rest):
    if first:
        out_ref, acc, sem = rest
        acc[...] = jnp.zeros(acc.shape, acc.dtype)
    else:
        acc_in, out_ref, acc, sem = rest
        load = pltpu.make_async_copy(acc_in, acc, sem)
        load.start()
        load.wait()

    def body(p, carry):
        a_block = a_ref[a_list[p]]
        b_block = b_ref[b_list[p]]
        product = lax.dot_general(
            a_block, b_block, (((1,), (1,)), ((), ())), preferred_element_type=jnp.float32
        )
        target = c_list[p]
        acc[target] = acc[target] + product
        return carry

    lax.fori_loop(0, count_ref[0], body, 0)

    if last:
        out_ref[...] = acc[...].astype(out_ref.dtype)
    else:
        store = pltpu.make_async_copy(acc, out_ref, sem)
        store.start()
        store.wait()


def run_tick(first, last, count, a_list, b_list, c_list, a_panel, b_panel, running, slots_c):
    block = a_panel.shape[1:]
    acc_shape = (slots_c,) + block
    in_specs = [
        pl.BlockSpec(a_panel.shape, lambda g, *_: (0, 0, 0)),
        pl.BlockSpec(b_panel.shape, lambda g, *_: (0, 0, 0)),
    ]
    operands = [count, a_list, b_list, c_list, a_panel, b_panel]
    aliases = {}
    if not first:
        in_specs.append(pl.BlockSpec(memory_space=pl.ANY))
        operands.append(running)
        if not last:
            aliases = {6: 0}
    if last:
        out_shape = jax.ShapeDtypeStruct(acc_shape, jnp.bfloat16)
        out_spec = pl.BlockSpec(acc_shape, lambda g, *_: (0, 0, 0))
    else:
        out_shape = jax.ShapeDtypeStruct(acc_shape, jnp.float32)
        out_spec = pl.BlockSpec(memory_space=pl.ANY)
    grid_spec = pltpu.PrefetchScalarGridSpec(
        num_scalar_prefetch=4,
        grid=(1,),
        in_specs=in_specs,
        out_specs=out_spec,
        scratch_shapes=[pltpu.VMEM(acc_shape, jnp.float32), pltpu.SemaphoreType.DMA],
    )
    return pl.pallas_call(
        functools.partial(tick_kernel, first, last),
        grid_spec=grid_spec,
        out_shape=out_shape,
        input_output_aliases=aliases,
    )(*operands)


def per_device(a_blocks, b_blocks, a_index, b_index, c_index, pair_count):
    row_index = lax.axis_index("row")
    col_index = lax.axis_index("col")
    row_count = lax.axis_size("row")
    col_count = lax.axis_size("col")
    tick_total = a_index.shape[2]
    back_reach = tick_total // 2 - 1
    slots_c = a_blocks.shape[2]
    a_own = a_blocks[0, 0]
    b_own = b_blocks[0, 0]
    order = sorted(range(tick_total), key=lambda t: (abs(t - back_reach), t < back_reach))
    running = None
    for step, tick in enumerate(order):
        offset = tick - back_reach
        if (-offset) % row_count == 0:
            a_panel = a_own
        else:
            a_panel = passed_along(a_own, "row", -offset)
        receiver_col = (col_index - offset) % col_count
        half_index = (row_index + receiver_col + offset) % row_count // col_count
        b_half = lax.dynamic_index_in_dim(b_own, half_index, 0, keepdims=False)
        if (-offset) % col_count == 0:
            b_panel = b_half
        else:
            b_panel = passed_along(b_half, "col", -offset)
        running = run_tick(
            step == 0,
            step == tick_total - 1,
            pair_count[0, 0, tick : tick + 1],
            a_index[0, 0, tick],
            b_index[0, 0, tick],
            c_index[0, 0, tick],
            a_panel,
            b_panel,
            running,
            slots_c,
        )
    return running[None, None]


def solution(mesh):
    placed = (
        P("row", "col", None, None, None),
        P("row", "col", None, None, None, None),
        P("row", "col", None, None),
        P("row", "col", None, None),
        P("row", "col", None, None),
        P("row", "col", None),
    )
    return jax.shard_map(
        per_device,
        mesh=mesh,
        in_specs=placed,
        out_specs=P("row", "col", None, None, None),
        check_vma=False,
    )
```
